128 devices in a mesh: region: 8 (over x, core), unit: 16 (over y, z).
Axes of the slice: x: 4, y: 4, z: 4, core: 2. Of those that a mesh axis runs over, the one named last changes fastest.
Arguments:
- noisy: bfloat16 [32768, 2048], P(('region', 'unit')), may hold values from -6 to 6
- strategy: bfloat16 [2048, 2048], replicated, may hold values from -0.125 to 0.125
- county_hist: float32 [1024, 2048], P(('region', 'unit')), may hold values from -24 to 24
- tract_county: int32 [32768], P(('region', 'unit')), may hold values from 0 to 1023, as said below
- tract_owner: int32 [32768, 1], P(('region', 'unit')), may hold values from 0 to 127; in each aligned block of 256 rows (0 to 255, 256 to 511, ...) at most 4 rows name the same one
Outputs:
- released: bfloat16 [32768, 2048], P(('region', 'unit'))
- relaid: float32 [65536, 2048], P(('region', 'unit'))
The draws below stay inside these ranges and needn't reach their ends.
Inputs may be any that keep to these rules, and one draw needn't show every extreme that they name: `tract_county`: every county has at least one tract; the tracts of region r (rows r * 256 * 16 onward) lie in counties of region r (rows r * 8 * 16 onward of county_hist). `tract_owner`: among the 256 rows of one device no owner appears more than 4 times, and some owner appears exactly 4 times.
All inputs are finite; a program needn't handle non-finite values.
Results may differ from the reference program's by a relative error of at most 0.005.
Values sent between devices are 32-bit elements; how exact they have to be, the bound alone decides.
No kernel may reach another device: no remote copies, remote signals or barrier semaphores. Data moves between devices by JAX's collectives and lax.ppermute only.
A program may use at most 64 MiB of HBM per device.

```python
import math
import jax
import jax.numpy as jnp
import numpy as np
from jax import lax

H = 2048
K = 2048
TR_DEV = 256
CTY_DEV = 8
ITERS = 2
TRACTS = 32768
COUNTIES = 1024
CAP = 4
N_REGION = 8
N_UNIT = 16
DEVICES = 128


def draw_tract_county(key, part):
    tract_region = TR_DEV * N_UNIT
    county_region = CTY_DEV * N_UNIT

    def region_draw(region_key):
        first_key, second_key, third_key = jax.random.split(region_key, 3)
        order_rank = jax.random.permutation(first_key, tract_region)
        left_pick = jax.random.randint(second_key, (tract_region,), 0, county_region)
        right_pick = jax.random.randint(third_key, (tract_region,), 0, county_region)
        skewed = jnp.minimum(left_pick, right_pick)
        return jnp.where(order_rank < county_region, order_rank, skewed).astype(jnp.int32)
    region_keys = jax.random.split(jax.random.fold_in(key, 17), N_REGION)
    local_ids = jax.vmap(region_draw)(region_keys)
    offsets = (jnp.arange(N_REGION, dtype=jnp.int32) * county_region)[:, None]
    return (local_ids + offsets).reshape(-1).astype(jnp.int32)


def levels(rng, shape, pieces, least, largest):
    loudness = 1.0
    for position, blocks in pieces:
        steps = jax.random.uniform(jax.random.fold_in(jax.random.fold_in(rng, 6), position), (blocks,), jnp.float32, least / len(pieces), largest / len(pieces))
        loudness = loudness * jnp.repeat(jnp.exp(steps), shape[position] // blocks).reshape((-1,) + (1,) * (len(shape) - 1 - position))
    return loudness


def deal_out(own_key, own, number, rows, amount, top, reach, skew):
    order = jax.random.permutation(own_key, amount)
    crowded, common = shares(amount, rows * top, reach, skew, True), shares(amount, rows * top, reach, skew, False)
    places = jnp.arange(amount)

    def named(sizes, turn):
        used = int((sizes > 0).sum())
        fixed = max(1, used // 4)
        shifted = fixed + (places - fixed + turn * (used - fixed)) % max(1, amount - fixed)
        return jnp.zeros((amount,), jnp.int32).at[order[jnp.where(places < fixed, places, shifted)]].set(jnp.asarray(sizes, jnp.int32))

    sizes = jnp.where(number % 4 == 0, named(crowded, number // 4), named(common, number - number // 4 - 1))
    mixed = jax.random.permutation(jax.random.fold_in(own, 3), amount)
    donor, receiver = mixed[0:amount // 2 * 2:2], mixed[1:amount // 2 * 2:2]
    room = jnp.minimum(sizes[donor] - 1, reach - sizes[receiver]) // 2
    room = jnp.where((donor == order[0]) | (receiver == order[0]) | (sizes[receiver] == 0), 0, jnp.maximum(room, 0))
    shifted = jax.random.randint(jax.random.fold_in(own, 4), (amount // 2,), 0, 1 << 20) % (room + 1)
    sizes = sizes.at[donor].add(-shifted).at[receiver].add(shifted)
    members = jnp.searchsorted(jnp.cumsum(sizes), jnp.arange(rows * top), side="right").astype(jnp.int32)
    table = members.reshape(top, rows).T
    table = table[jax.random.permutation(jax.random.fold_in(own, 1), rows)]
    turn = jax.random.randint(jax.random.fold_in(own, 2), (rows, 1), 0, top)
    return jnp.take_along_axis(table, (jnp.arange(top)[None, :] + turn) % top, axis=1)


def shares(count, total, most, lean, full):
    weights = [(1 << 20) // math.isqrt(grade ** lean) + 1 for grade in range(1, count + 1)]
    largest = most if full else min(most, max(-(-total // count), total * weights[0] // sum(weights)))
    least = 1 if total - largest >= count - 1 else 0
    counts, rest = [largest] + [least] * (count - 1), total - largest - least * (count - 1)
    while rest > 0:
        free = [i for i in range(1, count) if counts[i] < largest] or [i for i in range(1, count) if counts[i] < most]
        pool, remaining = sum([weights[i] for i in free]), rest
        for i in free:
            addition = min(most - counts[i], max(1, remaining * weights[i] // pool), rest)
            counts[i] = counts[i] + addition
            rest = rest - addition
    return np.array(counts)


def normal_values(key, shape, deviation, limit, cuts=(), held_as=jnp.bfloat16):
    values = jax.random.normal(key, shape, jnp.float32) * deviation
    if len(cuts) > 0:
        values = levels(key, shape, cuts, -0.22, 0.18) * values
    return jnp.clip(values, min=-limit, max=limit).astype(held_as)


def setup_inputs(seed: int = 0) -> dict:
    key_of = jax.random.split(jax.random.key(seed), 6)
    noisy = normal_values(key_of[0], (TRACTS, K), 1.0, 6.0, ((0, 128),))
    strategy = normal_values(key_of[1], (H, K), H ** -0.5, 0.125)
    county_hist = normal_values(key_of[2], (COUNTIES, H), 4.0, 24.0, ((0, 128),), jnp.float32)
    tract_county = draw_tract_county(jax.random.fold_in(key_of[5], 71), 0)
    tract_owner_keys = jax.random.split(jax.random.fold_in(key_of[4], 1), TRACTS // TR_DEV)
    tract_owner_turns = jax.random.permutation(jax.random.fold_in(key_of[4], 3), TRACTS // TR_DEV)
    tract_owner = jax.vmap(lambda own, number: deal_out(jax.random.fold_in(key_of[4], 2), own, number, TR_DEV, DEVICES, 1, CAP, 2))(tract_owner_keys, tract_owner_turns).reshape((TRACTS, 1))
    return dict(noisy=noisy, strategy=strategy, county_hist=county_hist, tract_county=tract_county, tract_owner=tract_owner)


step_size = 0.25


def reference(noisy, strategy, county_hist, tract_county, tract_owner):
    tracts = noisy.shape[0]
    tract_count = jax.ops.segment_sum(jnp.ones((tracts,), jnp.float32), tract_county, num_segments=COUNTIES)
    estimate = jnp.zeros((tracts, H), jnp.float32)
    for iteration in range(ITERS):
        answers = jnp.dot(estimate.astype(jnp.bfloat16), strategy, preferred_element_type=jnp.float32)
        misfit = (answers - noisy.astype(jnp.float32)).astype(jnp.bfloat16)
        gradient = lax.dot_general(misfit, strategy, (((1,), (1,)), ((), ())), preferred_element_type=jnp.float32)
        stepped = estimate - step_size * gradient
        child_total = jax.ops.segment_sum(stepped, tract_county, num_segments=COUNTIES)
        parent_gap = (county_hist - child_total) / tract_count[:, None]
        estimate = stepped + parent_gap[tract_county]
    released = jnp.dot(estimate.astype(jnp.bfloat16), strategy, preferred_element_type=jnp.float32).astype(jnp.bfloat16)
    owners = tract_owner[:, 0].reshape(DEVICES, TR_DEV)
    owner_hits = (owners[:, :, None] == jnp.arange(DEVICES, dtype=jnp.int32)[None, None, :]).astype(jnp.int32)
    slot_index = jnp.sum((jnp.cumsum(owner_hits, axis=1) - owner_hits) * owner_hits, axis=2)
    source = jnp.arange(DEVICES, dtype=jnp.int32)[:, None]
    target = (owners * (DEVICES * CAP) + source * CAP + slot_index).astype(jnp.int32)
    relaid = jnp.zeros((DEVICES * DEVICES * CAP, H), jnp.float32).at[target.reshape(-1)].set(estimate)
    return released, relaid
```

```python
import jax
import jax.numpy as jnp
from jax import lax
from jax.sharding import PartitionSpec as P

ITERS = 2


step_size = 0.25


def unit_sum(partial, unit_count):
    rows, cols = partial.shape
    grouped = partial.reshape(unit_count, rows // unit_count, cols)
    arrived = lax.all_to_all(grouped, "unit", 0, 0, tiled=True)
    return jnp.sum(arrived, axis=0)


def unit_gather(block, unit_count):
    spread = jnp.broadcast_to(block[None], (unit_count,) + block.shape)
    arrived = lax.all_to_all(spread, "unit", 0, 0, tiled=True)
    return arrived.reshape(unit_count * block.shape[0], block.shape[1])


def local(noisy, strategy, county_hist, tract_county, tract_owner):
    unit_count = lax.axis_size("unit")
    region_count = lax.axis_size("region")
    devices = region_count * unit_count
    tract_rows = noisy.shape[0]
    width = strategy.shape[0]
    county_region = county_hist.shape[0] * unit_count
    first_county = lax.axis_index("region") * county_region
    local_id = tract_county - first_county
    member = (local_id[:, None] == jnp.arange(county_region, dtype=jnp.int32)[None, :]).astype(
        jnp.float32
    )
    county_tally = jnp.sum(member, axis=0)
    tally_lanes = 128
    estimate = jnp.zeros((tract_rows, width), jnp.float32)
    tract_count = None
    for iteration in range(ITERS):
        if iteration == 0:
            misfit = -noisy
        else:
            answers = jnp.dot(
                estimate.astype(jnp.bfloat16), strategy, preferred_element_type=jnp.float32
            )
            misfit = (answers - noisy.astype(jnp.float32)).astype(jnp.bfloat16)
        gradient = lax.dot_general(
            misfit, strategy, (((1,), (1,)), ((), ())), preferred_element_type=jnp.float32
        )
        stepped = estimate - step_size * gradient
        partial_value = lax.dot_general(
            member,
            stepped,
            (((0,), (0,)), ((), ())),
            precision=lax.Precision.HIGHEST,
            preferred_element_type=jnp.float32,
        )
        if tract_count is None:
            tally = jnp.broadcast_to(county_tally[:, None], (county_region, tally_lanes))
            summed = unit_sum(jnp.concatenate([partial_value, tally], axis=1), unit_count)
            child_total = summed[:, :width]
            tract_count = summed[:, width]
        else:
            child_total = unit_sum(partial_value, unit_count)
        parent_gap = (county_hist - child_total) / tract_count[:, None]
        region_gap = unit_gather(parent_gap, unit_count)
        estimate = stepped + jnp.dot(
            member, region_gap, precision=lax.Precision.HIGHEST, preferred_element_type=jnp.float32
        )
    owners = tract_owner[:, 0]
    owner_hits = (owners[:, None] == jnp.arange(devices, dtype=jnp.int32)[None, :]).astype(
        jnp.int32
    )
    slot_index = jnp.sum((jnp.cumsum(owner_hits, axis=0) - owner_hits) * owner_hits, axis=1)
    capacity = 2 * tract_rows // devices
    target = owners * capacity + slot_index
    outgoing = jnp.zeros((devices * capacity, width), jnp.float32).at[target].set(estimate)
    released = jnp.dot(
        estimate.astype(jnp.bfloat16), strategy, preferred_element_type=jnp.float32
    ).astype(jnp.bfloat16)
    grouped = outgoing.reshape(devices, capacity, width)
    arrived = lax.all_to_all(grouped, ("region", "unit"), split_axis=0, concat_axis=0, tiled=True)
    relaid = arrived.reshape(devices * capacity, width)
    return (released, relaid)


def solution(mesh):
    in_specs = (
        P(("region", "unit"), None),
        P(),
        P(("region", "unit"), None),
        P(("region", "unit")),
        P(("region", "unit"), None),
    )
    out_specs = (P(("region", "unit"), None), P(("region", "unit"), None))
    return jax.shard_map(local, mesh=mesh, in_specs=in_specs, out_specs=out_specs, check_vma=False)
```

```python
import jax
import jax.numpy as jnp
from jax import lax
from jax.sharding import PartitionSpec as P

ITERS = 2


step_size = 0.25


def unit_sum(partial, unit_count):
    rows, cols = partial.shape
    grouped = partial.reshape(unit_count, rows // unit_count, cols)
    arrived = lax.all_to_all(grouped, "unit", 0, 0, tiled=True)
    return jnp.sum(arrived, axis=0)


def unit_gather(block, unit_count):
    spread = jnp.broadcast_to(block[None], (unit_count,) + block.shape)
    arrived = lax.all_to_all(spread, "unit", 0, 0, tiled=True)
    return arrived.reshape(unit_count * block.shape[0], block.shape[1])


def local(noisy, strategy, county_hist, tract_county, tract_owner):
    unit_count = lax.axis_size("unit")
    region_count = lax.axis_size("region")
    devices = region_count * unit_count
    tract_rows = noisy.shape[0]
    width = strategy.shape[0]
    county_region = county_hist.shape[0] * unit_count
    first_county = lax.axis_index("region") * county_region
    local_id = tract_county - first_county
    member = (local_id[:, None] == jnp.arange(county_region, dtype=jnp.int32)[None, :]).astype(
        jnp.float32
    )
    county_tally = jnp.sum(member, axis=0)
    tally_lanes = 128
    estimate = jnp.zeros((tract_rows, width), jnp.float32)
    tract_count = None
    for iteration in range(ITERS):
        if iteration == 0:
            misfit = -noisy
        else:
            answers = jnp.dot(
                estimate.astype(jnp.bfloat16), strategy, preferred_element_type=jnp.float32
            )
            misfit = (answers - noisy.astype(jnp.float32)).astype(jnp.bfloat16)
        gradient = lax.dot_general(
            misfit, strategy, (((1,), (1,)), ((), ())), preferred_element_type=jnp.float32
        )
        stepped = estimate - step_size * gradient
        partial_value = lax.dot_general(
            member,
            stepped,
            (((0,), (0,)), ((), ())),
            precision=lax.Precision.HIGHEST,
            preferred_element_type=jnp.float32,
        )
        if tract_count is None:
            tally = jnp.broadcast_to(county_tally[:, None], (county_region, tally_lanes))
            summed = unit_sum(jnp.concatenate([partial_value, tally], axis=1), unit_count)
            child_total = summed[:, :width]
            tract_count = summed[:, width]
        else:
            child_total = unit_sum(partial_value, unit_count)
        parent_gap = (county_hist - child_total) / tract_count[:, None]
        region_gap = unit_gather(parent_gap, unit_count)
        estimate = stepped + jnp.take(region_gap, local_id, axis=0)
    owners = tract_owner[:, 0]
    owner_hits = (owners[:, None] == jnp.arange(devices, dtype=jnp.int32)[None, :]).astype(
        jnp.int32
    )
    slot_index = jnp.sum((jnp.cumsum(owner_hits, axis=0) - owner_hits) * owner_hits, axis=1)
    capacity = 2 * tract_rows // devices
    outgoing = jnp.zeros((devices, capacity, width), jnp.float32).at[owners, slot_index].set(
        estimate
    )
    released = jnp.dot(
        estimate.astype(jnp.bfloat16), strategy, preferred_element_type=jnp.float32
    ).astype(jnp.bfloat16)
    arrived = lax.all_to_all(outgoing, ("region", "unit"), split_axis=0, concat_axis=0, tiled=True)
    relaid = arrived.reshape(devices * capacity, width)
    return (released, relaid)


def solution(mesh):
    in_specs = (
        P(("region", "unit"), None),
        P(),
        P(("region", "unit"), None),
        P(("region", "unit")),
        P(("region", "unit"), None),
    )
    out_specs = (P(("region", "unit"), None), P(("region", "unit"), None))
    return jax.shard_map(local, mesh=mesh, in_specs=in_specs, out_specs=out_specs, check_vma=False)
```

```python
import jax
import jax.numpy as jnp
from jax import lax
from jax.experimental import pallas as pl
from jax.sharding import PartitionSpec as P

ITERS = 2


step_size = 0.25


COLUMN_BLOCK = 1024


def _answer_kernel(e_ref, s_ref, n_ref, o_ref):
    answers = jnp.dot(e_ref[...], s_ref[...], preferred_element_type=jnp.float32)
    o_ref[...] = (answers - n_ref[...].astype(jnp.float32)).astype(o_ref.dtype)


def misfit_of(estimate_bf16, strategy, noisy):
    rows, inner = estimate_bf16.shape
    cols = strategy.shape[1]
    block = min(COLUMN_BLOCK, cols)
    return pl.pallas_call(
        _answer_kernel,
        grid=(cols // block,),
        in_specs=[
            pl.BlockSpec((rows, inner), lambda j: (0, 0)),
            pl.BlockSpec((inner, block), lambda j: (0, j)),
            pl.BlockSpec((rows, block), lambda j: (0, j)),
        ],
        out_specs=pl.BlockSpec((rows, block), lambda j: (0, j)),
        out_shape=jax.ShapeDtypeStruct((rows, cols), jnp.bfloat16),
        cost_estimate=pl.CostEstimate(
            flops=2 * rows * inner * cols,
            transcendentals=0,
            bytes_accessed=2 * (rows * inner + inner * cols + 2 * rows * cols),
        ),
    )(estimate_bf16, strategy, noisy)


def _step_kernel(m_ref, s_ref, e_ref, o_ref):
    gradient = lax.dot_general(
        m_ref[...], s_ref[...], (((1,), (1,)), ((), ())), preferred_element_type=jnp.float32
    )
    o_ref[...] = e_ref[...] - step_size * gradient


def _first_step_kernel(m_ref, s_ref, o_ref):
    gradient = lax.dot_general(
        m_ref[...], s_ref[...], (((1,), (1,)), ((), ())), preferred_element_type=jnp.float32
    )
    o_ref[...] = 0.0 - step_size * gradient


def stepped_of(misfit, strategy, estimate):
    rows, inner = misfit.shape
    cols = strategy.shape[0]
    block = min(COLUMN_BLOCK, cols)
    in_specs = [
        pl.BlockSpec((rows, inner), lambda j: (0, 0)),
        pl.BlockSpec((block, inner), lambda j: (j, 0)),
    ]
    operands = [misfit, strategy]
    kernel = _first_step_kernel
    if estimate is not None:
        in_specs.append(pl.BlockSpec((rows, block), lambda j: (0, j)))
        operands.append(estimate)
        kernel = _step_kernel
    return pl.pallas_call(
        kernel,
        grid=(cols // block,),
        in_specs=in_specs,
        out_specs=pl.BlockSpec((rows, block), lambda j: (0, j)),
        out_shape=jax.ShapeDtypeStruct((rows, cols), jnp.float32),
        cost_estimate=pl.CostEstimate(
            flops=2 * rows * inner * cols,
            transcendentals=0,
            bytes_accessed=2 * (rows * inner + inner * cols) + 8 * rows * cols,
        ),
    )(*operands)


def unit_sum(partial, unit_count):
    rows, cols = partial.shape
    grouped = partial.reshape(unit_count, rows // unit_count, cols)
    arrived = lax.all_to_all(grouped, "unit", 0, 0, tiled=True)
    return jnp.sum(arrived, axis=0)


def unit_gather(block, unit_count):
    spread = jnp.broadcast_to(block[None], (unit_count,) + block.shape)
    arrived = lax.all_to_all(spread, "unit", 0, 0, tiled=True)
    return arrived.reshape(unit_count * block.shape[0], block.shape[1])


def local(noisy, strategy, county_hist, tract_county, tract_owner):
    unit_count = lax.axis_size("unit")
    region_count = lax.axis_size("region")
    devices = region_count * unit_count
    tract_rows = noisy.shape[0]
    width = strategy.shape[0]
    county_region = county_hist.shape[0] * unit_count
    first_county = lax.axis_index("region") * county_region
    local_id = tract_county - first_county
    member = (local_id[:, None] == jnp.arange(county_region, dtype=jnp.int32)[None, :]).astype(
        jnp.float32
    )
    county_tally = jnp.sum(member, axis=0)
    tally_lanes = 128
    estimate = jnp.zeros((tract_rows, width), jnp.float32)
    tract_count = None
    for iteration in range(ITERS):
        if iteration == 0:
            stepped = stepped_of(-noisy, strategy, None)
        else:
            misfit = misfit_of(estimate.astype(jnp.bfloat16), strategy, noisy)
            stepped = stepped_of(misfit, strategy, estimate)
        partial_value = lax.dot_general(
            member,
            stepped,
            (((0,), (0,)), ((), ())),
            precision=lax.Precision.HIGH,
            preferred_element_type=jnp.float32,
        )
        if tract_count is None:
            tally = jnp.broadcast_to(county_tally[:, None], (county_region, tally_lanes))
            summed = unit_sum(jnp.concatenate([partial_value, tally], axis=1), unit_count)
            child_total = summed[:, :width]
            tract_count = summed[:, width]
        else:
            child_total = unit_sum(partial_value, unit_count)
        parent_gap = (county_hist - child_total) / tract_count[:, None]
        region_gap = unit_gather(parent_gap, unit_count)
        estimate = stepped + jnp.dot(
            member, region_gap, precision=lax.Precision.HIGH, preferred_element_type=jnp.float32
        )
    owners = tract_owner[:, 0]
    owner_hits = (owners[:, None] == jnp.arange(devices, dtype=jnp.int32)[None, :]).astype(
        jnp.int32
    )
    slot_index = jnp.sum((jnp.cumsum(owner_hits, axis=0) - owner_hits) * owner_hits, axis=1)
    capacity = 2 * tract_rows // devices
    target = owners * capacity + slot_index
    outgoing = jnp.zeros((devices * capacity, width), jnp.float32).at[target].set(estimate)
    released = jnp.dot(
        estimate.astype(jnp.bfloat16), strategy, preferred_element_type=jnp.float32
    ).astype(jnp.bfloat16)
    grouped = outgoing.reshape(devices, capacity, width)
    arrived = lax.all_to_all(grouped, ("region", "unit"), split_axis=0, concat_axis=0, tiled=True)
    relaid = arrived.reshape(devices * capacity, width)
    return (released, relaid)


def solution(mesh):
    in_specs = (
        P(("region", "unit"), None),
        P(),
        P(("region", "unit"), None),
        P(("region", "unit")),
        P(("region", "unit"), None),
    )
    out_specs = (P(("region", "unit"), None), P(("region", "unit"), None))
    return jax.shard_map(local, mesh=mesh, in_specs=in_specs, out_specs=out_specs, check_vma=False)
```

```python
import jax
import jax.numpy as jnp
from jax import lax
from jax.sharding import PartitionSpec as P

ITERS = 2


step_size = 0.25


def unit_sum(partial, unit_count):
    rows, cols = partial.shape
    grouped = partial.reshape(unit_count, rows // unit_count, cols)
    arrived = lax.all_to_all(grouped, "unit", 0, 0, tiled=True)
    return jnp.sum(arrived, axis=0)


def unit_gather(block, unit_count):
    spread = jnp.broadcast_to(block[None], (unit_count,) + block.shape)
    arrived = lax.all_to_all(spread, "unit", 0, 0, tiled=True)
    return arrived.reshape(unit_count * block.shape[0], block.shape[1])


def local(noisy, strategy, county_hist, tract_county, tract_owner):
    unit_count = lax.axis_size("unit")
    region_count = lax.axis_size("region")
    devices = region_count * unit_count
    tract_rows = noisy.shape[0]
    width = strategy.shape[0]
    county_region = county_hist.shape[0] * unit_count
    first_county = lax.axis_index("region") * county_region
    local_id = tract_county - first_county
    member = (local_id[:, None] == jnp.arange(county_region, dtype=jnp.int32)[None, :]).astype(
        jnp.float32
    )
    county_tally = jnp.sum(member, axis=0)
    tally_lanes = 128
    owners = tract_owner[:, 0]
    owner_hits = (owners[:, None] == jnp.arange(devices, dtype=jnp.int32)[None, :]).astype(
        jnp.int32
    )
    slot_index = jnp.sum((jnp.cumsum(owner_hits, axis=0) - owner_hits) * owner_hits, axis=1)
    capacity = 2 * tract_rows // devices
    target = owners * capacity + slot_index
    slot_hits = target[None, :] == jnp.arange(devices * capacity, dtype=jnp.int32)[:, None]
    slot_county = jnp.sum(jnp.where(slot_hits, local_id[None, :] + 1, 0), axis=1) - 1
    slot_member = (
        slot_county[:, None] == jnp.arange(county_region, dtype=jnp.int32)[None, :]
    ).astype(jnp.float32).reshape(devices, capacity, county_region)
    estimate = jnp.zeros((tract_rows, width), jnp.float32)
    tract_count = None
    for iteration in range(ITERS):
        if iteration == 0:
            misfit = -noisy
        else:
            answers = jnp.dot(
                estimate.astype(jnp.bfloat16), strategy, preferred_element_type=jnp.float32
            )
            misfit = (answers - noisy.astype(jnp.float32)).astype(jnp.bfloat16)
        gradient = lax.dot_general(
            misfit, strategy, (((1,), (1,)), ((), ())), preferred_element_type=jnp.float32
        )
        stepped = estimate - step_size * gradient
        partial_value = lax.dot_general(
            member,
            stepped,
            (((0,), (0,)), ((), ())),
            precision=lax.Precision.HIGHEST,
            preferred_element_type=jnp.float32,
        )
        if tract_count is None:
            tally = jnp.broadcast_to(county_tally[:, None], (county_region, tally_lanes))
            summed = unit_sum(jnp.concatenate([partial_value, tally], axis=1), unit_count)
            child_total = summed[:, :width]
            tract_count = summed[:, width]
        else:
            child_total = unit_sum(partial_value, unit_count)
        if iteration == ITERS - 1:
            slot_stepped = (
                jnp.zeros((devices * capacity, width), jnp.float32)
                .at[target]
                .set(stepped)
                .reshape(devices, capacity, width)
            )
        parent_gap = (county_hist - child_total) / tract_count[:, None]
        region_gap = unit_gather(parent_gap, unit_count)
        estimate = stepped + jnp.dot(
            member, region_gap, precision=lax.Precision.HIGHEST, preferred_element_type=jnp.float32
        )
    grouped = slot_stepped + jnp.einsum(
        "osc,ch->osh",
        slot_member,
        region_gap,
        precision=lax.Precision.HIGHEST,
        preferred_element_type=jnp.float32,
    )
    released = jnp.dot(
        estimate.astype(jnp.bfloat16), strategy, preferred_element_type=jnp.float32
    ).astype(jnp.bfloat16)
    arrived = lax.all_to_all(grouped, ("region", "unit"), split_axis=0, concat_axis=0, tiled=True)
    relaid = arrived.reshape(devices * capacity, width)
    return (released, relaid)


def solution(mesh):
    in_specs = (
        P(("region", "unit"), None),
        P(),
        P(("region", "unit"), None),
        P(("region", "unit")),
        P(("region", "unit"), None),
    )
    out_specs = (P(("region", "unit"), None), P(("region", "unit"), None))
    return jax.shard_map(local, mesh=mesh, in_specs=in_specs, out_specs=out_specs, check_vma=False)
```

```python
import jax
import jax.numpy as jnp
from jax import lax
from jax.sharding import PartitionSpec as P

ITERS = 2


step_size = 0.25


def bf16_pieces(value):
    high = lax.reduce_precision(value, exponent_bits=8, mantissa_bits=7)
    rest = value - high
    middle = lax.reduce_precision(rest, exponent_bits=8, mantissa_bits=7)
    low = rest - middle
    return jnp.concatenate(
        [high.astype(jnp.bfloat16), middle.astype(jnp.bfloat16), low.astype(jnp.bfloat16)], axis=0
    )


def one_hot_pick(selector, table_pieces):
    stacked = jnp.concatenate([selector.astype(jnp.bfloat16)] * 3, axis=-1)
    return jnp.einsum("...k,kh->...h", stacked, table_pieces, preferred_element_type=jnp.float32)


def unit_sum(partial, unit_count):
    rows, cols = partial.shape
    grouped = partial.reshape(unit_count, rows // unit_count, cols)
    arrived = lax.all_to_all(grouped, "unit", 0, 0, tiled=True)
    return jnp.sum(arrived, axis=0)


def unit_gather(block, unit_count):
    spread = jnp.broadcast_to(block[None], (unit_count,) + block.shape)
    arrived = lax.all_to_all(spread, "unit", 0, 0, tiled=True)
    return arrived.reshape(unit_count * block.shape[0], block.shape[1])


def local(noisy, strategy, county_hist, tract_county, tract_owner):
    unit_count = lax.axis_size("unit")
    region_count = lax.axis_size("region")
    devices = region_count * unit_count
    tract_rows = noisy.shape[0]
    width = strategy.shape[0]
    county_region = county_hist.shape[0] * unit_count
    first_county = lax.axis_index("region") * county_region
    local_id = tract_county - first_county
    member = (local_id[:, None] == jnp.arange(county_region, dtype=jnp.int32)[None, :]).astype(
        jnp.float32
    )
    county_tally = jnp.sum(member, axis=0)
    tally_lanes = 128
    owners = tract_owner[:, 0]
    owner_hits = (owners[:, None] == jnp.arange(devices, dtype=jnp.int32)[None, :]).astype(
        jnp.int32
    )
    slot_index = jnp.sum((jnp.cumsum(owner_hits, axis=0) - owner_hits) * owner_hits, axis=1)
    capacity = 2 * tract_rows // devices
    target = owners * capacity + slot_index
    slot_hits = target[None, :] == jnp.arange(devices * capacity, dtype=jnp.int32)[:, None]
    slot_county = jnp.sum(jnp.where(slot_hits, local_id[None, :] + 1, 0), axis=1) - 1
    slot_member = (
        slot_county[:, None] == jnp.arange(county_region, dtype=jnp.int32)[None, :]
    ).astype(jnp.float32).reshape(devices, capacity, county_region)
    estimate = jnp.zeros((tract_rows, width), jnp.float32)
    tract_count = None
    for iteration in range(ITERS):
        if iteration == 0:
            misfit = -noisy
        else:
            answers = jnp.dot(
                estimate.astype(jnp.bfloat16), strategy, preferred_element_type=jnp.float32
            )
            misfit = (answers - noisy.astype(jnp.float32)).astype(jnp.bfloat16)
        gradient = lax.dot_general(
            misfit, strategy, (((1,), (1,)), ((), ())), preferred_element_type=jnp.float32
        )
        stepped = estimate - step_size * gradient
        partial_value = lax.dot_general(
            member,
            stepped,
            (((0,), (0,)), ((), ())),
            precision=lax.Precision.HIGHEST,
            preferred_element_type=jnp.float32,
        )
        if tract_count is None:
            tally = jnp.broadcast_to(county_tally[:, None], (county_region, tally_lanes))
            summed = unit_sum(jnp.concatenate([partial_value, tally], axis=1), unit_count)
            child_total = summed[:, :width]
            tract_count = summed[:, width]
        else:
            child_total = unit_sum(partial_value, unit_count)
        if iteration == ITERS - 1:
            slot_stepped = (
                jnp.zeros((devices * capacity, width), jnp.float32)
                .at[target]
                .set(stepped)
                .reshape(devices, capacity, width)
            )
        parent_gap = (county_hist - child_total) / tract_count[:, None]
        region_gap = unit_gather(parent_gap, unit_count)
        gap_pieces = bf16_pieces(region_gap)
        estimate = stepped + one_hot_pick(member, gap_pieces)
    grouped = slot_stepped + one_hot_pick(slot_member, gap_pieces)
    released = jnp.dot(
        estimate.astype(jnp.bfloat16), strategy, preferred_element_type=jnp.float32
    ).astype(jnp.bfloat16)
    arrived = lax.all_to_all(grouped, ("region", "unit"), split_axis=0, concat_axis=0, tiled=True)
    relaid = arrived.reshape(devices * capacity, width)
    return (released, relaid)


def solution(mesh):
    in_specs = (
        P(("region", "unit"), None),
        P(),
        P(("region", "unit"), None),
        P(("region", "unit")),
        P(("region", "unit"), None),
    )
    out_specs = (P(("region", "unit"), None), P(("region", "unit"), None))
    return jax.shard_map(local, mesh=mesh, in_specs=in_specs, out_specs=out_specs, check_vma=False)
```

```python
import jax
import jax.numpy as jnp
from jax import lax
from jax.sharding import PartitionSpec as P

ITERS = 2


step_size = 0.25


def bf16_pieces(value):
    high = lax.reduce_precision(value, exponent_bits=8, mantissa_bits=7)
    rest = value - high
    middle = lax.reduce_precision(rest, exponent_bits=8, mantissa_bits=7)
    low = rest - middle
    return jnp.concatenate(
        [high.astype(jnp.bfloat16), middle.astype(jnp.bfloat16), low.astype(jnp.bfloat16)], axis=0
    )


def one_hot_pick(selector, table_pieces):
    stacked = jnp.concatenate([selector.astype(jnp.bfloat16)] * 3, axis=-1)
    return jnp.einsum("...k,kh->...h", stacked, table_pieces, preferred_element_type=jnp.float32)


def unit_sum(partial, unit_count):
    rows, cols = partial.shape
    grouped = partial.reshape(unit_count, rows // unit_count, cols)
    arrived = lax.all_to_all(grouped, "unit", 0, 0, tiled=True)
    return jnp.sum(arrived, axis=0)


def unit_gather(block, unit_count):
    spread = jnp.broadcast_to(block[None], (unit_count,) + block.shape)
    arrived = lax.all_to_all(spread, "unit", 0, 0, tiled=True)
    return arrived.reshape(unit_count * block.shape[0], block.shape[1])


def local(noisy, strategy, county_hist, tract_county, tract_owner):
    unit_count = lax.axis_size("unit")
    region_count = lax.axis_size("region")
    devices = region_count * unit_count
    tract_rows = noisy.shape[0]
    width = strategy.shape[0]
    county_region = county_hist.shape[0] * unit_count
    first_county = lax.axis_index("region") * county_region
    local_id = tract_county - first_county
    member = (local_id[:, None] == jnp.arange(county_region, dtype=jnp.int32)[None, :]).astype(
        jnp.float32
    )
    county_tally = jnp.sum(member, axis=0)
    tally_lanes = 128
    owners = tract_owner[:, 0]
    owner_hits = (owners[:, None] == jnp.arange(devices, dtype=jnp.int32)[None, :]).astype(
        jnp.int32
    )
    slot_index = jnp.sum((jnp.cumsum(owner_hits, axis=0) - owner_hits) * owner_hits, axis=1)
    capacity = 2 * tract_rows // devices
    target = owners * capacity + slot_index
    slot_hits = target[None, :] == jnp.arange(devices * capacity, dtype=jnp.int32)[:, None]
    slot_county = jnp.sum(jnp.where(slot_hits, local_id[None, :] + 1, 0), axis=1) - 1
    slot_member = (
        slot_county[:, None] == jnp.arange(county_region, dtype=jnp.int32)[None, :]
    ).astype(jnp.float32).reshape(devices, capacity, county_region)
    tally = jnp.broadcast_to(county_tally[:, None], (county_region, tally_lanes))
    tract_count = unit_sum(tally, unit_count)[:, 0]
    estimate = jnp.zeros((tract_rows, width), jnp.float32)
    for iteration in range(ITERS):
        if iteration == 0:
            misfit = -noisy
        else:
            answers = jnp.dot(
                estimate.astype(jnp.bfloat16), strategy, preferred_element_type=jnp.float32
            )
            misfit = (answers - noisy.astype(jnp.float32)).astype(jnp.bfloat16)
        gradient = lax.dot_general(
            misfit, strategy, (((1,), (1,)), ((), ())), preferred_element_type=jnp.float32
        )
        stepped = estimate - step_size * gradient
        partial_value = lax.dot_general(
            member,
            stepped,
            (((0,), (0,)), ((), ())),
            precision=lax.Precision.HIGHEST,
            preferred_element_type=jnp.float32,
        )
        child_total = unit_sum(partial_value, unit_count)
        if iteration == ITERS - 1:
            slot_stepped = (
                jnp.zeros((devices * capacity, width), jnp.float32)
                .at[target]
                .set(stepped)
                .reshape(devices, capacity, width)
            )
        parent_gap = (county_hist - child_total) / tract_count[:, None]
        region_gap = unit_gather(parent_gap, unit_count)
        gap_pieces = bf16_pieces(region_gap)
        estimate = stepped + one_hot_pick(member, gap_pieces)
    grouped = slot_stepped + one_hot_pick(slot_member, gap_pieces)
    released = jnp.dot(
        estimate.astype(jnp.bfloat16), strategy, preferred_element_type=jnp.float32
    ).astype(jnp.bfloat16)
    arrived = lax.all_to_all(grouped, ("region", "unit"), split_axis=0, concat_axis=0, tiled=True)
    relaid = arrived.reshape(devices * capacity, width)
    return (released, relaid)


def solution(mesh):
    in_specs = (
        P(("region", "unit"), None),
        P(),
        P(("region", "unit"), None),
        P(("region", "unit")),
        P(("region", "unit"), None),
    )
    out_specs = (P(("region", "unit"), None), P(("region", "unit"), None))
    return jax.shard_map(local, mesh=mesh, in_specs=in_specs, out_specs=out_specs, check_vma=False)
```

```python
import jax
import jax.numpy as jnp
from jax import lax
from jax.sharding import PartitionSpec as P

ITERS = 2


step_size = 0.25


def bf16_pieces(value):
    high = lax.reduce_precision(value, exponent_bits=8, mantissa_bits=7)
    rest = value - high
    middle = lax.reduce_precision(rest, exponent_bits=8, mantissa_bits=7)
    low = rest - middle
    return jnp.concatenate(
        [high.astype(jnp.bfloat16), middle.astype(jnp.bfloat16), low.astype(jnp.bfloat16)], axis=0
    )


def one_hot_pick(selector, table_pieces):
    stacked = jnp.concatenate([selector.astype(jnp.bfloat16)] * 3, axis=-1)
    return jnp.einsum("...k,kh->...h", stacked, table_pieces, preferred_element_type=jnp.float32)


def unit_sum(partial, unit_count):
    rows, cols = partial.shape
    grouped = partial.reshape(unit_count, rows // unit_count, cols)
    arrived = lax.all_to_all(grouped, "unit", 0, 0, tiled=True)
    return jnp.sum(arrived, axis=0)


def unit_gather(block, unit_count):
    spread = jnp.broadcast_to(block[None], (unit_count,) + block.shape)
    arrived = lax.all_to_all(spread, "unit", 0, 0, tiled=True)
    return arrived.reshape(unit_count * block.shape[0], block.shape[1])


def local(noisy, strategy, county_hist, tract_county, tract_owner):
    unit_count = lax.axis_size("unit")
    region_count = lax.axis_size("region")
    devices = region_count * unit_count
    tract_rows = noisy.shape[0]
    width = strategy.shape[0]
    county_region = county_hist.shape[0] * unit_count
    first_county = lax.axis_index("region") * county_region
    local_id = tract_county - first_county
    member = (local_id[:, None] == jnp.arange(county_region, dtype=jnp.int32)[None, :]).astype(
        jnp.float32
    )
    county_tally = jnp.sum(member, axis=0)
    tally_lanes = 128
    estimate = jnp.zeros((tract_rows, width), jnp.float32)
    tract_count = None
    for iteration in range(ITERS):
        if iteration == 0:
            misfit = -noisy
        else:
            answers = jnp.dot(
                estimate.astype(jnp.bfloat16), strategy, preferred_element_type=jnp.float32
            )
            misfit = (answers - noisy.astype(jnp.float32)).astype(jnp.bfloat16)
        gradient = lax.dot_general(
            misfit, strategy, (((1,), (1,)), ((), ())), preferred_element_type=jnp.float32
        )
        stepped = estimate - step_size * gradient
        partial_value = lax.dot_general(
            member,
            stepped,
            (((0,), (0,)), ((), ())),
            precision=lax.Precision.HIGHEST,
            preferred_element_type=jnp.float32,
        )
        if tract_count is None:
            tally = jnp.broadcast_to(county_tally[:, None], (county_region, tally_lanes))
            summed = unit_sum(jnp.concatenate([partial_value, tally], axis=1), unit_count)
            child_total = summed[:, :width]
            tract_count = summed[:, width]
        else:
            child_total = unit_sum(partial_value, unit_count)
        if iteration == ITERS - 1:
            late_owner, child_total = lax.optimization_barrier((tract_owner, child_total))
            owners = late_owner[:, 0]
            owner_hits = (
                owners[:, None] == jnp.arange(devices, dtype=jnp.int32)[None, :]
            ).astype(jnp.int32)
            slot_index = jnp.sum(
                (jnp.cumsum(owner_hits, axis=0) - owner_hits) * owner_hits, axis=1
            )
            capacity = 2 * tract_rows // devices
            target = owners * capacity + slot_index
            slot_hits = (
                target[None, :] == jnp.arange(devices * capacity, dtype=jnp.int32)[:, None]
            )
            slot_county = jnp.sum(jnp.where(slot_hits, local_id[None, :] + 1, 0), axis=1) - 1
            slot_member = (
                slot_county[:, None] == jnp.arange(county_region, dtype=jnp.int32)[None, :]
            ).astype(jnp.float32).reshape(devices, capacity, county_region)
            slot_stepped = (
                jnp.zeros((devices * capacity, width), jnp.float32)
                .at[target]
                .set(stepped)
                .reshape(devices, capacity, width)
            )
        parent_gap = (county_hist - child_total) / tract_count[:, None]
        region_gap = unit_gather(parent_gap, unit_count)
        gap_pieces = bf16_pieces(region_gap)
        estimate = stepped + one_hot_pick(member, gap_pieces)
    grouped = slot_stepped + one_hot_pick(slot_member, gap_pieces)
    released = jnp.dot(
        estimate.astype(jnp.bfloat16), strategy, preferred_element_type=jnp.float32
    ).astype(jnp.bfloat16)
    arrived = lax.all_to_all(grouped, ("region", "unit"), split_axis=0, concat_axis=0, tiled=True)
    relaid = arrived.reshape(devices * capacity, width)
    return (released, relaid)


def solution(mesh):
    in_specs = (
        P(("region", "unit"), None),
        P(),
        P(("region", "unit"), None),
        P(("region", "unit")),
        P(("region", "unit"), None),
    )
    out_specs = (P(("region", "unit"), None), P(("region", "unit"), None))
    return jax.shard_map(local, mesh=mesh, in_specs=in_specs, out_specs=out_specs, check_vma=False)
```

```python
import jax
import jax.numpy as jnp
from jax import lax
from jax.sharding import PartitionSpec as P

ITERS = 2


step_size = 0.25


def unit_sum(partial, unit_count):
    rows, cols = partial.shape
    grouped = partial.reshape(unit_count, rows // unit_count, cols)
    arrived = lax.all_to_all(grouped, "unit", 0, 0, tiled=True)
    return jnp.sum(arrived, axis=0)


def unit_gather(block, unit_count):
    spread = jnp.broadcast_to(block[None], (unit_count,) + block.shape)
    arrived = lax.all_to_all(spread, "unit", 0, 0, tiled=True)
    return arrived.reshape(unit_count * block.shape[0], block.shape[1])


def local(noisy, strategy, county_hist, tract_county, tract_owner):
    unit_count = lax.axis_size("unit")
    region_count = lax.axis_size("region")
    devices = region_count * unit_count
    tract_rows = noisy.shape[0]
    width = strategy.shape[0]
    county_region = county_hist.shape[0] * unit_count
    first_county = lax.axis_index("region") * county_region
    local_id = tract_county - first_county
    member = (local_id[:, None] == jnp.arange(county_region, dtype=jnp.int32)[None, :]).astype(
        jnp.float32
    )
    county_tally = jnp.sum(member, axis=0)
    tally_lanes = 128
    estimate = jnp.zeros((tract_rows, width), jnp.float32)
    tract_count = None
    for iteration in range(ITERS):
        if iteration == 0:
            misfit = -noisy
        else:
            answers = jnp.dot(
                estimate.astype(jnp.bfloat16), strategy, preferred_element_type=jnp.float32
            )
            misfit = (answers - noisy.astype(jnp.float32)).astype(jnp.bfloat16)
        gradient = lax.dot_general(
            misfit, strategy, (((1,), (1,)), ((), ())), preferred_element_type=jnp.float32
        )
        stepped = estimate - step_size * gradient
        partial_value = lax.dot_general(
            member,
            stepped,
            (((0,), (0,)), ((), ())),
            precision=lax.Precision.HIGHEST,
            preferred_element_type=jnp.float32,
        )
        if tract_count is None:
            tally = jnp.broadcast_to(county_tally[:, None], (county_region, tally_lanes))
            summed = unit_sum(jnp.concatenate([partial_value, tally], axis=1), unit_count)
            child_total = summed[:, :width]
            tract_count = summed[:, width]
        else:
            child_total = unit_sum(partial_value, unit_count)
        if iteration == ITERS - 1:
            late_owner, child_total = lax.optimization_barrier((tract_owner, child_total))
            owners = late_owner[:, 0]
            owner_hits = (
                owners[:, None] == jnp.arange(devices, dtype=jnp.int32)[None, :]
            ).astype(jnp.int32)
            slot_index = jnp.sum(
                (jnp.cumsum(owner_hits, axis=0) - owner_hits) * owner_hits, axis=1
            )
            capacity = 2 * tract_rows // devices
            target = owners * capacity + slot_index
            slot_hits = (
                target[None, :] == jnp.arange(devices * capacity, dtype=jnp.int32)[:, None]
            )
            slot_county = jnp.sum(jnp.where(slot_hits, local_id[None, :] + 1, 0), axis=1) - 1
            slot_member = (
                slot_county[:, None] == jnp.arange(county_region, dtype=jnp.int32)[None, :]
            ).astype(jnp.float32).reshape(devices, capacity, county_region)
            slot_stepped = (
                jnp.zeros((devices * capacity, width), jnp.float32)
                .at[target]
                .set(stepped)
                .reshape(devices, capacity, width)
            )
        parent_gap = (county_hist - child_total) / tract_count[:, None]
        region_gap = unit_gather(parent_gap, unit_count)
        estimate = stepped + jnp.dot(
            member, region_gap, precision=lax.Precision.HIGHEST, preferred_element_type=jnp.float32
        )
    grouped = slot_stepped + jnp.einsum(
        "osc,ch->osh",
        slot_member,
        region_gap,
        precision=lax.Precision.HIGHEST,
        preferred_element_type=jnp.float32,
    )
    released = jnp.dot(
        estimate.astype(jnp.bfloat16), strategy, preferred_element_type=jnp.float32
    ).astype(jnp.bfloat16)
    arrived = lax.all_to_all(grouped, ("region", "unit"), split_axis=0, concat_axis=0, tiled=True)
    relaid = arrived.reshape(devices * capacity, width)
    return (released, relaid)


def solution(mesh):
    in_specs = (
        P(("region", "unit"), None),
        P(),
        P(("region", "unit"), None),
        P(("region", "unit")),
        P(("region", "unit"), None),
    )
    out_specs = (P(("region", "unit"), None), P(("region", "unit"), None))
    return jax.shard_map(local, mesh=mesh, in_specs=in_specs, out_specs=out_specs, check_vma=False)
```

```python
import jax
import jax.numpy as jnp
from jax import lax
from jax.sharding import PartitionSpec as P

ITERS = 2


step_size = 0.25


def bf16_pieces(value):
    high = lax.reduce_precision(value, exponent_bits=8, mantissa_bits=7)
    rest = value - high
    middle = lax.reduce_precision(rest, exponent_bits=8, mantissa_bits=7)
    low = rest - middle
    return jnp.concatenate(
        [high.astype(jnp.bfloat16), middle.astype(jnp.bfloat16), low.astype(jnp.bfloat16)], axis=0
    )


def one_hot_pick(selector, table_pieces):
    stacked = jnp.concatenate([selector.astype(jnp.bfloat16)] * 3, axis=-1)
    return jnp.einsum("...k,kh->...h", stacked, table_pieces, preferred_element_type=jnp.float32)


def unit_sum(partial, unit_count):
    rows, cols = partial.shape
    grouped = partial.reshape(unit_count, rows // unit_count, cols)
    arrived = lax.all_to_all(grouped, "unit", 0, 0, tiled=True)
    return jnp.sum(arrived, axis=0)


def unit_gather(block, unit_count):
    spread = jnp.broadcast_to(block[None], (unit_count,) + block.shape)
    arrived = lax.all_to_all(spread, "unit", 0, 0, tiled=True)
    return arrived.reshape(unit_count * block.shape[0], block.shape[1])


def local(noisy, strategy, county_hist, tract_county, tract_owner):
    unit_count = lax.axis_size("unit")
    region_count = lax.axis_size("region")
    devices = region_count * unit_count
    tract_rows = noisy.shape[0]
    width = strategy.shape[0]
    county_region = county_hist.shape[0] * unit_count
    first_county = lax.axis_index("region") * county_region
    local_id = tract_county - first_county
    member = (local_id[:, None] == jnp.arange(county_region, dtype=jnp.int32)[None, :]).astype(
        jnp.float32
    )
    county_tally = jnp.sum(member, axis=0)
    tally_lanes = 128
    estimate = jnp.zeros((tract_rows, width), jnp.float32)
    tract_count = None
    for iteration in range(ITERS):
        if iteration == 0:
            misfit = -noisy
        else:
            answers = jnp.dot(
                estimate.astype(jnp.bfloat16), strategy, preferred_element_type=jnp.float32
            )
            misfit = (answers - noisy.astype(jnp.float32)).astype(jnp.bfloat16)
        gradient = lax.dot_general(
            misfit, strategy, (((1,), (1,)), ((), ())), preferred_element_type=jnp.float32
        )
        stepped = estimate - step_size * gradient
        partial_value = lax.dot_general(
            member,
            stepped,
            (((0,), (0,)), ((), ())),
            precision=lax.Precision.HIGHEST,
            preferred_element_type=jnp.float32,
        )
        if tract_count is None:
            tally = jnp.broadcast_to(county_tally[:, None], (county_region, tally_lanes))
            summed = unit_sum(jnp.concatenate([partial_value, tally], axis=1), unit_count)
            child_total = summed[:, :width]
            tract_count = summed[:, width]
        else:
            child_total = unit_sum(partial_value, unit_count)
        if iteration == ITERS - 1:
            late_owner, child_total = lax.optimization_barrier((tract_owner, child_total))
            owners = late_owner[:, 0]
            owner_hits = (
                owners[:, None] == jnp.arange(devices, dtype=jnp.int32)[None, :]
            ).astype(jnp.int32)
            slot_index = jnp.sum(
                (jnp.cumsum(owner_hits, axis=0) - owner_hits) * owner_hits, axis=1
            )
            capacity = 2 * tract_rows // devices
            target = owners * capacity + slot_index
            slot_hits = (
                target[None, :] == jnp.arange(devices * capacity, dtype=jnp.int32)[:, None]
            )
            slot_county = jnp.sum(jnp.where(slot_hits, local_id[None, :] + 1, 0), axis=1) - 1
            slot_member = (
                slot_county[:, None] == jnp.arange(county_region, dtype=jnp.int32)[None, :]
            ).astype(jnp.float32).reshape(devices, capacity, county_region)
            slot_stepped = (
                jnp.zeros((devices * capacity, width), jnp.float32)
                .at[target]
                .set(stepped)
                .reshape(devices, capacity, width)
            )
        parent_gap = (county_hist - child_total) / tract_count[:, None]
        region_gap = unit_gather(parent_gap, unit_count)
        estimate = stepped + jnp.dot(
            member, region_gap, precision=lax.Precision.HIGHEST, preferred_element_type=jnp.float32
        )
    grouped = slot_stepped + one_hot_pick(slot_member, bf16_pieces(region_gap))
    released = jnp.dot(
        estimate.astype(jnp.bfloat16), strategy, preferred_element_type=jnp.float32
    ).astype(jnp.bfloat16)
    arrived = lax.all_to_all(grouped, ("region", "unit"), split_axis=0, concat_axis=0, tiled=True)
    relaid = arrived.reshape(devices * capacity, width)
    return (released, relaid)


def solution(mesh):
    in_specs = (
        P(("region", "unit"), None),
        P(),
        P(("region", "unit"), None),
        P(("region", "unit")),
        P(("region", "unit"), None),
    )
    out_specs = (P(("region", "unit"), None), P(("region", "unit"), None))
    return jax.shard_map(local, mesh=mesh, in_specs=in_specs, out_specs=out_specs, check_vma=False)
```

```python
import jax
import jax.numpy as jnp
from jax import lax
from jax.sharding import PartitionSpec as P

ITERS = 2


step_size = 0.25


def bf16_pieces(value):
    high = lax.reduce_precision(value, exponent_bits=8, mantissa_bits=7)
    rest = value - high
    middle = lax.reduce_precision(rest, exponent_bits=8, mantissa_bits=7)
    low = rest - middle
    return jnp.concatenate(
        [high.astype(jnp.bfloat16), middle.astype(jnp.bfloat16), low.astype(jnp.bfloat16)], axis=0
    )


def one_hot_pick(selector, table_pieces):
    stacked = jnp.concatenate([selector.astype(jnp.bfloat16)] * 3, axis=-1)
    return jnp.einsum("...k,kh->...h", stacked, table_pieces, preferred_element_type=jnp.float32)


def unit_sum(partial, unit_count):
    rows, cols = partial.shape
    grouped = partial.reshape(unit_count, rows // unit_count, cols)
    arrived = lax.all_to_all(grouped, "unit", 0, 0, tiled=True)
    return jnp.sum(arrived, axis=0)


def unit_gather(block, unit_count):
    spread = jnp.broadcast_to(block[None], (unit_count,) + block.shape)
    arrived = lax.all_to_all(spread, "unit", 0, 0, tiled=True)
    return arrived.reshape(unit_count * block.shape[0], block.shape[1])


def local(noisy, strategy, county_hist, tract_county, tract_owner):
    unit_count = lax.axis_size("unit")
    region_count = lax.axis_size("region")
    devices = region_count * unit_count
    tract_rows = noisy.shape[0]
    width = strategy.shape[0]
    county_region = county_hist.shape[0] * unit_count
    first_county = lax.axis_index("region") * county_region
    local_id = tract_county - first_county
    member = (local_id[:, None] == jnp.arange(county_region, dtype=jnp.int32)[None, :]).astype(
        jnp.float32
    )
    county_tally = jnp.sum(member, axis=0)
    tally_lanes = 128
    estimate = jnp.zeros((tract_rows, width), jnp.float32)
    tract_count = None
    for iteration in range(ITERS):
        if iteration == 0:
            misfit = -noisy
        else:
            answers = jnp.dot(
                estimate.astype(jnp.bfloat16), strategy, preferred_element_type=jnp.float32
            )
            misfit = (answers - noisy.astype(jnp.float32)).astype(jnp.bfloat16)
        gradient = lax.dot_general(
            misfit, strategy, (((1,), (1,)), ((), ())), preferred_element_type=jnp.float32
        )
        stepped = estimate - step_size * gradient
        partial_value = lax.dot_general(
            member,
            stepped,
            (((0,), (0,)), ((), ())),
            precision=lax.Precision.HIGHEST,
            preferred_element_type=jnp.float32,
        )
        if tract_count is None:
            tally = jnp.broadcast_to(county_tally[:, None], (county_region, tally_lanes))
            summed = unit_sum(jnp.concatenate([partial_value, tally], axis=1), unit_count)
            child_total = summed[:, :width]
            tract_count = summed[:, width]
        else:
            child_total = unit_sum(partial_value, unit_count)
        if iteration == ITERS - 1:
            late_owner, child_total = lax.optimization_barrier((tract_owner, child_total))
            owners = late_owner[:, 0]
            owner_hits = (
                owners[:, None] == jnp.arange(devices, dtype=jnp.int32)[None, :]
            ).astype(jnp.int32)
            slot_index = jnp.sum(
                (jnp.cumsum(owner_hits, axis=0) - owner_hits) * owner_hits, axis=1
            )
            capacity = 2 * tract_rows // devices
            target = owners * capacity + slot_index
            slot_hits = (
                target[None, :] == jnp.arange(devices * capacity, dtype=jnp.int32)[:, None]
            )
            slot_county = jnp.sum(jnp.where(slot_hits, local_id[None, :] + 1, 0), axis=1) - 1
            half = width // 2
            row_county = jnp.repeat(slot_county, 2)
            row_half = jnp.tile(jnp.arange(2, dtype=jnp.int32), devices * capacity)
            k = jnp.arange(2 * 3 * county_region, dtype=jnp.int32)[None, :]
            row_pick = (
                (k // (3 * county_region) == row_half[:, None])
                & (k % county_region == row_county[:, None])
            ).astype(jnp.bfloat16)
            slot_stepped = (
                jnp.zeros((devices * capacity, width), jnp.float32)
                .at[target]
                .set(stepped)
                .reshape(devices, 2 * capacity, half)
            )
        parent_gap = (county_hist - child_total) / tract_count[:, None]
        region_gap = unit_gather(parent_gap, unit_count)
        estimate = stepped + jnp.dot(
            member, region_gap, precision=lax.Precision.HIGHEST, preferred_element_type=jnp.float32
        )
    gap_pieces = bf16_pieces(region_gap)
    halves = jnp.concatenate([gap_pieces[:, :half], gap_pieces[:, half:]], axis=0)
    picked = jnp.dot(row_pick, halves, preferred_element_type=jnp.float32)
    grouped = slot_stepped + picked.reshape(devices, 2 * capacity, half)
    released = jnp.dot(
        estimate.astype(jnp.bfloat16), strategy, preferred_element_type=jnp.float32
    ).astype(jnp.bfloat16)
    arrived = lax.all_to_all(grouped, ("region", "unit"), split_axis=0, concat_axis=0, tiled=True)
    relaid = arrived.reshape(devices * capacity, width)
    return (released, relaid)


def solution(mesh):
    in_specs = (
        P(("region", "unit"), None),
        P(),
        P(("region", "unit"), None),
        P(("region", "unit")),
        P(("region", "unit"), None),
    )
    out_specs = (P(("region", "unit"), None), P(("region", "unit"), None))
    return jax.shard_map(local, mesh=mesh, in_specs=in_specs, out_specs=out_specs, check_vma=False)
```

```python
import jax
import jax.numpy as jnp
from jax import lax
from jax.sharding import PartitionSpec as P

ITERS = 2


step_size = 0.25


def bf16_pieces(value):
    high = lax.reduce_precision(value, exponent_bits=8, mantissa_bits=7)
    rest = value - high
    middle = lax.reduce_precision(rest, exponent_bits=8, mantissa_bits=7)
    low = rest - middle
    return jnp.concatenate(
        [high.astype(jnp.bfloat16), middle.astype(jnp.bfloat16), low.astype(jnp.bfloat16)], axis=0
    )


def one_hot_pick(selector, table_pieces):
    stacked = jnp.concatenate([selector.astype(jnp.bfloat16)] * 3, axis=-1)
    return jnp.einsum("...k,kh->...h", stacked, table_pieces, preferred_element_type=jnp.float32)


def unit_sum(partial, unit_count):
    rows, cols = partial.shape
    grouped = partial.reshape(unit_count, rows // unit_count, cols)
    arrived = lax.all_to_all(grouped, "unit", 0, 0, tiled=True)
    return jnp.sum(arrived, axis=0)


def unit_gather(block, unit_count):
    spread = jnp.broadcast_to(block[None], (unit_count,) + block.shape)
    arrived = lax.all_to_all(spread, "unit", 0, 0, tiled=True)
    return arrived.reshape(unit_count * block.shape[0], block.shape[1])


def local(noisy, strategy, county_hist, tract_county, tract_owner):
    unit_count = lax.axis_size("unit")
    region_count = lax.axis_size("region")
    devices = region_count * unit_count
    tract_rows = noisy.shape[0]
    width = strategy.shape[0]
    county_region = county_hist.shape[0] * unit_count
    first_county = lax.axis_index("region") * county_region
    local_id = tract_county - first_county
    member = (local_id[:, None] == jnp.arange(county_region, dtype=jnp.int32)[None, :]).astype(
        jnp.float32
    )
    county_tally = jnp.sum(member, axis=0)
    tally_lanes = 128
    estimate = jnp.zeros((tract_rows, width), jnp.float32)
    tract_count = None
    for iteration in range(ITERS):
        if iteration == 0:
            misfit = -noisy
        else:
            answers = jnp.dot(
                estimate.astype(jnp.bfloat16), strategy, preferred_element_type=jnp.float32
            )
            misfit = (answers - noisy.astype(jnp.float32)).astype(jnp.bfloat16)
        gradient = lax.dot_general(
            misfit, strategy, (((1,), (1,)), ((), ())), preferred_element_type=jnp.float32
        )
        stepped = estimate - step_size * gradient
        partial_value = lax.dot_general(
            member,
            stepped,
            (((0,), (0,)), ((), ())),
            precision=lax.Precision.HIGHEST,
            preferred_element_type=jnp.float32,
        )
        if tract_count is None:
            tally = jnp.broadcast_to(county_tally[:, None], (county_region, tally_lanes))
            summed = unit_sum(jnp.concatenate([partial_value, tally], axis=1), unit_count)
            child_total = summed[:, :width]
            tract_count = summed[:, width]
        else:
            child_total = unit_sum(partial_value, unit_count)
        if iteration == ITERS - 1:
            late_owner, child_total = lax.optimization_barrier((tract_owner, child_total))
            owners = late_owner[:, 0]
            owner_hits = (
                owners[:, None] == jnp.arange(devices, dtype=jnp.int32)[None, :]
            ).astype(jnp.int32)
            slot_index = jnp.sum(
                (jnp.cumsum(owner_hits, axis=0) - owner_hits) * owner_hits, axis=1
            )
            capacity = 2 * tract_rows // devices
            target = owners * capacity + slot_index
            slot_hits = (
                target[None, :] == jnp.arange(devices * capacity, dtype=jnp.int32)[:, None]
            )
            slot_county = jnp.sum(jnp.where(slot_hits, local_id[None, :] + 1, 0), axis=1) - 1
            half = width // 2
            row_county = jnp.repeat(slot_county, 2)
            row_half = jnp.tile(jnp.arange(2, dtype=jnp.int32), devices * capacity)
            k = jnp.arange(2 * 3 * county_region, dtype=jnp.int32)[None, :]
            row_pick = (
                (k // (3 * county_region) == row_half[:, None])
                & (k % county_region == row_county[:, None])
            ).astype(jnp.bfloat16)
            half_target = (2 * target[:, None] + jnp.arange(2, dtype=jnp.int32)[None, :]).reshape(-1)
            slot_stepped = (
                jnp.zeros((2 * devices * capacity, half), jnp.float32)
                .at[half_target]
                .set(stepped.reshape(2 * tract_rows, half))
                .reshape(devices, 2 * capacity, half)
            )
        parent_gap = (county_hist - child_total) / tract_count[:, None]
        region_gap = unit_gather(parent_gap, unit_count)
        estimate = stepped + jnp.dot(
            member, region_gap, precision=lax.Precision.HIGHEST, preferred_element_type=jnp.float32
        )
    gap_pieces = bf16_pieces(region_gap)
    halves = jnp.concatenate([gap_pieces[:, :half], gap_pieces[:, half:]], axis=0)
    picked = jnp.dot(row_pick, halves, preferred_element_type=jnp.float32)
    grouped = slot_stepped + picked.reshape(devices, 2 * capacity, half)
    released = jnp.dot(
        estimate.astype(jnp.bfloat16), strategy, preferred_element_type=jnp.float32
    ).astype(jnp.bfloat16)
    arrived = lax.all_to_all(grouped, ("region", "unit"), split_axis=0, concat_axis=0, tiled=True)
    relaid = arrived.reshape(devices * capacity, width)
    return (released, relaid)


def solution(mesh):
    in_specs = (
        P(("region", "unit"), None),
        P(),
        P(("region", "unit"), None),
        P(("region", "unit")),
        P(("region", "unit"), None),
    )
    out_specs = (P(("region", "unit"), None), P(("region", "unit"), None))
    return jax.shard_map(local, mesh=mesh, in_specs=in_specs, out_specs=out_specs, check_vma=False)
```

```python
import jax
import jax.numpy as jnp
from jax import lax
from jax.sharding import PartitionSpec as P

ITERS = 2


step_size = 0.25


def bf16_pieces(value):
    high = lax.reduce_precision(value, exponent_bits=8, mantissa_bits=7)
    rest = value - high
    middle = lax.reduce_precision(rest, exponent_bits=8, mantissa_bits=7)
    low = rest - middle
    return jnp.concatenate(
        [high.astype(jnp.bfloat16), middle.astype(jnp.bfloat16), low.astype(jnp.bfloat16)], axis=0
    )


def one_hot_pick(selector, table_pieces):
    stacked = jnp.concatenate([selector.astype(jnp.bfloat16)] * 3, axis=-1)
    return jnp.einsum("...k,kh->...h", stacked, table_pieces, preferred_element_type=jnp.float32)


def unit_sum(partial, unit_count):
    rows, cols = partial.shape
    grouped = partial.reshape(unit_count, rows // unit_count, cols)
    arrived = lax.all_to_all(grouped, "unit", 0, 0, tiled=True)
    return jnp.sum(arrived, axis=0)


def unit_gather(block, unit_count):
    spread = jnp.broadcast_to(block[None], (unit_count,) + block.shape)
    arrived = lax.all_to_all(spread, "unit", 0, 0, tiled=True)
    return arrived.reshape(unit_count * block.shape[0], block.shape[1])


def local(noisy, strategy, county_hist, tract_county, tract_owner):
    unit_count = lax.axis_size("unit")
    region_count = lax.axis_size("region")
    devices = region_count * unit_count
    tract_rows = noisy.shape[0]
    width = strategy.shape[0]
    county_region = county_hist.shape[0] * unit_count
    first_county = lax.axis_index("region") * county_region
    local_id = tract_county - first_county
    member = (local_id[:, None] == jnp.arange(county_region, dtype=jnp.int32)[None, :]).astype(
        jnp.float32
    )
    county_tally = jnp.sum(member, axis=0)
    tally_lanes = 128
    estimate = jnp.zeros((tract_rows, width), jnp.float32)
    tract_count = None
    for iteration in range(ITERS):
        if iteration == 0:
            misfit = -noisy
        else:
            answers = jnp.dot(
                estimate.astype(jnp.bfloat16), strategy, preferred_element_type=jnp.float32
            )
            misfit = (answers - noisy.astype(jnp.float32)).astype(jnp.bfloat16)
        gradient = lax.dot_general(
            misfit, strategy, (((1,), (1,)), ((), ())), preferred_element_type=jnp.float32
        )
        stepped = estimate - step_size * gradient
        partial_value = lax.dot_general(
            member,
            stepped,
            (((0,), (0,)), ((), ())),
            precision=lax.Precision.HIGHEST,
            preferred_element_type=jnp.float32,
        )
        if tract_count is None:
            tally = jnp.broadcast_to(county_tally[:, None], (county_region, tally_lanes))
            summed = unit_sum(jnp.concatenate([partial_value, tally], axis=1), unit_count)
            child_total = summed[:, :width]
            tract_count = summed[:, width]
        else:
            child_total = unit_sum(partial_value, unit_count)
        if iteration == ITERS - 1:
            late_owner, late_stepped, child_total = lax.optimization_barrier(
                (tract_owner, stepped, child_total)
            )
            owners = late_owner[:, 0]
            owner_hits = (
                owners[:, None] == jnp.arange(devices, dtype=jnp.int32)[None, :]
            ).astype(jnp.int32)
            slot_index = jnp.sum(
                (jnp.cumsum(owner_hits, axis=0) - owner_hits) * owner_hits, axis=1
            )
            capacity = 2 * tract_rows // devices
            target = owners * capacity + slot_index
            slot_hits = (
                target[None, :] == jnp.arange(devices * capacity, dtype=jnp.int32)[:, None]
            )
            slot_county = jnp.sum(jnp.where(slot_hits, local_id[None, :] + 1, 0), axis=1) - 1
            half = width // 2
            row_county = jnp.repeat(slot_county, 2)
            pick_shape = (2 * devices * capacity, 2 * 3 * county_region)
            row = lax.broadcasted_iota(jnp.int32, pick_shape, 0)
            k = lax.broadcasted_iota(jnp.int32, pick_shape, 1)
            row_pick = (
                (k // (3 * county_region) == row % 2) & (k % county_region == row_county[:, None])
            ).astype(jnp.bfloat16)
            half_target = (2 * target[:, None] + jnp.arange(2, dtype=jnp.int32)[None, :]).reshape(-1)
            slot_stepped = (
                jnp.zeros((2 * devices * capacity, half), jnp.float32)
                .at[half_target]
                .set(late_stepped.reshape(2 * tract_rows, half))
                .reshape(devices, 2 * capacity, half)
            )
        parent_gap = (county_hist - child_total) / tract_count[:, None]
        region_gap = unit_gather(parent_gap, unit_count)
        estimate = stepped + jnp.dot(
            member, region_gap, precision=lax.Precision.HIGHEST, preferred_element_type=jnp.float32
        )
    gap_pieces = bf16_pieces(region_gap)
    halves = jnp.concatenate([gap_pieces[:, :half], gap_pieces[:, half:]], axis=0)
    picked = jnp.dot(row_pick, halves, preferred_element_type=jnp.float32)
    grouped = slot_stepped + picked.reshape(devices, 2 * capacity, half)
    released = jnp.dot(
        estimate.astype(jnp.bfloat16), strategy, preferred_element_type=jnp.float32
    ).astype(jnp.bfloat16)
    arrived = lax.all_to_all(grouped, ("region", "unit"), split_axis=0, concat_axis=0, tiled=True)
    relaid = arrived.reshape(devices * capacity, width)
    return (released, relaid)


def solution(mesh):
    in_specs = (
        P(("region", "unit"), None),
        P(),
        P(("region", "unit"), None),
        P(("region", "unit")),
        P(("region", "unit"), None),
    )
    out_specs = (P(("region", "unit"), None), P(("region", "unit"), None))
    return jax.shard_map(local, mesh=mesh, in_specs=in_specs, out_specs=out_specs, check_vma=False)
```

```python
import jax
import jax.numpy as jnp
from jax import lax
from jax.sharding import PartitionSpec as P

ITERS = 2


step_size = 0.25


def bf16_pieces(value):
    high = lax.reduce_precision(value, exponent_bits=8, mantissa_bits=7)
    rest = value - high
    middle = lax.reduce_precision(rest, exponent_bits=8, mantissa_bits=7)
    low = rest - middle
    return jnp.concatenate(
        [high.astype(jnp.bfloat16), middle.astype(jnp.bfloat16), low.astype(jnp.bfloat16)], axis=0
    )


def one_hot_pick(selector, table_pieces):
    stacked = jnp.concatenate([selector.astype(jnp.bfloat16)] * 3, axis=-1)
    return jnp.einsum("...k,kh->...h", stacked, table_pieces, preferred_element_type=jnp.float32)


def unit_sum(partial, unit_count):
    rows, cols = partial.shape
    grouped = partial.reshape(unit_count, rows // unit_count, cols)
    arrived = lax.all_to_all(grouped, "unit", 0, 0, tiled=True)
    return jnp.sum(arrived, axis=0)


def unit_gather(block, unit_count):
    spread = jnp.broadcast_to(block[None], (unit_count,) + block.shape)
    arrived = lax.all_to_all(spread, "unit", 0, 0, tiled=True)
    return arrived.reshape(unit_count * block.shape[0], block.shape[1])


def local(noisy, strategy, county_hist, tract_county, tract_owner):
    unit_count = lax.axis_size("unit")
    region_count = lax.axis_size("region")
    devices = region_count * unit_count
    tract_rows = noisy.shape[0]
    width = strategy.shape[0]
    county_region = county_hist.shape[0] * unit_count
    first_county = lax.axis_index("region") * county_region
    local_id = tract_county - first_county
    member_bf16 = (
        local_id[:, None] == jnp.arange(county_region, dtype=jnp.int32)[None, :]
    ).astype(jnp.bfloat16)
    member = member_bf16.astype(jnp.float32)
    county_tally = jnp.sum(member, axis=0)
    tally_lanes = 128
    estimate = jnp.zeros((tract_rows, width), jnp.float32)
    tract_count = None
    for iteration in range(ITERS):
        if iteration == 0:
            misfit = -noisy
        else:
            answers = jnp.dot(
                estimate.astype(jnp.bfloat16), strategy, preferred_element_type=jnp.float32
            )
            misfit = (answers - noisy.astype(jnp.float32)).astype(jnp.bfloat16)
        gradient = lax.dot_general(
            misfit, strategy, (((1,), (1,)), ((), ())), preferred_element_type=jnp.float32
        )
        stepped = estimate - step_size * gradient
        partial_value = lax.dot_general(
            member,
            stepped,
            (((0,), (0,)), ((), ())),
            precision=lax.Precision.HIGHEST,
            preferred_element_type=jnp.float32,
        )
        if tract_count is None:
            tally = jnp.broadcast_to(county_tally[:, None], (county_region, tally_lanes))
            summed = unit_sum(jnp.concatenate([partial_value, tally], axis=1), unit_count)
            child_total = summed[:, :width]
            tract_count = summed[:, width]
        else:
            child_total = unit_sum(partial_value, unit_count)
        if iteration == ITERS - 1:
            late_owner, child_total = lax.optimization_barrier((tract_owner, child_total))
            owners = late_owner[:, 0]
            owner_hits = (
                owners[:, None] == jnp.arange(devices, dtype=jnp.int32)[None, :]
            ).astype(jnp.int32)
            slot_index = jnp.sum(
                (jnp.cumsum(owner_hits, axis=0) - owner_hits) * owner_hits, axis=1
            )
            capacity = 2 * tract_rows // devices
            target = owners * capacity + slot_index
            slot_hits = (
                target[None, :] == jnp.arange(devices * capacity, dtype=jnp.int32)[:, None]
            )
            slot_county = jnp.sum(jnp.where(slot_hits, local_id[None, :] + 1, 0), axis=1) - 1
            slot_member = (
                slot_county[:, None] == jnp.arange(county_region, dtype=jnp.int32)[None, :]
            ).astype(jnp.float32).reshape(devices, capacity, county_region)
            slot_stepped = (
                jnp.zeros((devices * capacity, width), jnp.float32)
                .at[target]
                .set(stepped)
                .reshape(devices, capacity, width)
            )
        parent_gap = (county_hist - child_total) / tract_count[:, None]
        region_gap = unit_gather(parent_gap, unit_count)
        if iteration < ITERS - 1:
            pieces = bf16_pieces(region_gap).reshape(3, county_region, width)
            picks = [
                jnp.dot(member_bf16, piece, preferred_element_type=jnp.float32) for piece in pieces
            ]
            estimate = stepped + ((picks[0] + picks[1]) + picks[2])
        else:
            estimate = stepped + jnp.dot(
                member,
                region_gap,
                precision=lax.Precision.HIGHEST,
                preferred_element_type=jnp.float32,
            )
    grouped = slot_stepped + one_hot_pick(slot_member, bf16_pieces(region_gap))
    released = jnp.dot(
        estimate.astype(jnp.bfloat16), strategy, preferred_element_type=jnp.float32
    ).astype(jnp.bfloat16)
    arrived = lax.all_to_all(grouped, ("region", "unit"), split_axis=0, concat_axis=0, tiled=True)
    relaid = arrived.reshape(devices * capacity, width)
    return (released, relaid)


def solution(mesh):
    in_specs = (
        P(("region", "unit"), None),
        P(),
        P(("region", "unit"), None),
        P(("region", "unit")),
        P(("region", "unit"), None),
    )
    out_specs = (P(("region", "unit"), None), P(("region", "unit"), None))
    return jax.shard_map(local, mesh=mesh, in_specs=in_specs, out_specs=out_specs, check_vma=False)
```

```python
import jax
import jax.numpy as jnp
from jax import lax
from jax.sharding import PartitionSpec as P

ITERS = 2


step_size = 0.25


def bf16_pieces(value):
    high = lax.reduce_precision(value, exponent_bits=8, mantissa_bits=7)
    rest = value - high
    middle = lax.reduce_precision(rest, exponent_bits=8, mantissa_bits=7)
    low = rest - middle
    return jnp.concatenate(
        [high.astype(jnp.bfloat16), middle.astype(jnp.bfloat16), low.astype(jnp.bfloat16)], axis=0
    )


def one_hot_pick(selector, table_pieces):
    stacked = jnp.concatenate([selector.astype(jnp.bfloat16)] * 3, axis=-1)
    return jnp.einsum("...k,kh->...h", stacked, table_pieces, preferred_element_type=jnp.float32)


def unit_sum(partial, unit_count):
    rows, cols = partial.shape
    grouped = partial.reshape(unit_count, rows // unit_count, cols)
    arrived = lax.all_to_all(grouped, "unit", 0, 0, tiled=True)
    return jnp.sum(arrived, axis=0)


def unit_gather(block, unit_count):
    spread = jnp.broadcast_to(block[None], (unit_count,) + block.shape)
    arrived = lax.all_to_all(spread, "unit", 0, 0, tiled=True)
    return arrived.reshape(unit_count * block.shape[0], block.shape[1])


def local(noisy, strategy, county_hist, tract_county, tract_owner):
    unit_count = lax.axis_size("unit")
    region_count = lax.axis_size("region")
    devices = region_count * unit_count
    tract_rows = noisy.shape[0]
    width = strategy.shape[0]
    county_region = county_hist.shape[0] * unit_count
    first_county = lax.axis_index("region") * county_region
    local_id = tract_county - first_county
    member = (local_id[:, None] == jnp.arange(county_region, dtype=jnp.int32)[None, :]).astype(
        jnp.float32
    )
    county_tally = jnp.sum(member, axis=0)
    tally_lanes = 128
    estimate = jnp.zeros((tract_rows, width), jnp.float32)
    tract_count = None
    for iteration in range(ITERS):
        if iteration == 0:
            misfit = -noisy
        else:
            answers = jnp.dot(
                estimate.astype(jnp.bfloat16), strategy, preferred_element_type=jnp.float32
            )
            misfit = (answers - noisy.astype(jnp.float32)).astype(jnp.bfloat16)
        gradient = lax.dot_general(
            misfit, strategy, (((1,), (1,)), ((), ())), preferred_element_type=jnp.float32
        )
        stepped = estimate - step_size * gradient
        partial_value = lax.dot_general(
            member,
            stepped,
            (((0,), (0,)), ((), ())),
            precision=lax.Precision.HIGHEST,
            preferred_element_type=jnp.float32,
        )
        if tract_count is None:
            tally = jnp.broadcast_to(county_tally[:, None], (county_region, tally_lanes))
            summed = unit_sum(jnp.concatenate([partial_value, tally], axis=1), unit_count)
            child_total = summed[:, :width]
            tract_count = summed[:, width]
        else:
            child_total = unit_sum(partial_value, unit_count)
        if iteration == ITERS - 1:
            late_owner, child_total = lax.optimization_barrier((tract_owner, child_total))
            owners = late_owner[:, 0]
            owner_hits = (
                owners[:, None] == jnp.arange(devices, dtype=jnp.int32)[None, :]
            ).astype(jnp.int32)
            slot_index = jnp.sum(
                (jnp.cumsum(owner_hits, axis=0) - owner_hits) * owner_hits, axis=1
            )
            capacity = 2 * tract_rows // devices
            target = owners * capacity + slot_index
            slot_hits = (
                target[None, :] == jnp.arange(devices * capacity, dtype=jnp.int32)[:, None]
            )
            slot_county = jnp.sum(jnp.where(slot_hits, local_id[None, :] + 1, 0), axis=1) - 1
            half = width // 2
            row_county = jnp.repeat(slot_county, 2)
            pick_shape = (2 * devices * capacity, 2 * 3 * county_region)
            after = jnp.minimum(owners[0], 0)
            row = lax.broadcasted_iota(jnp.int32, pick_shape, 0) + after
            k = lax.broadcasted_iota(jnp.int32, pick_shape, 1) + after
            row_pick = (
                (k // (3 * county_region) == row % 2) & (k % county_region == row_county[:, None])
            ).astype(jnp.bfloat16)
            slot_stepped = (
                jnp.zeros((devices * capacity, width), jnp.float32)
                .at[target]
                .set(stepped)
                .reshape(devices, 2 * capacity, half)
            )
        parent_gap = (county_hist - child_total) / tract_count[:, None]
        region_gap = unit_gather(parent_gap, unit_count)
        estimate = stepped + jnp.dot(
            member, region_gap, precision=lax.Precision.HIGHEST, preferred_element_type=jnp.float32
        )
    gap_pieces = bf16_pieces(region_gap)
    halves = jnp.concatenate([gap_pieces[:, :half], gap_pieces[:, half:]], axis=0)
    picked = jnp.dot(row_pick, halves, preferred_element_type=jnp.float32)
    grouped = slot_stepped + picked.reshape(devices, 2 * capacity, half)
    released = jnp.dot(
        estimate.astype(jnp.bfloat16), strategy, preferred_element_type=jnp.float32
    ).astype(jnp.bfloat16)
    arrived = lax.all_to_all(grouped, ("region", "unit"), split_axis=0, concat_axis=0, tiled=True)
    relaid = arrived.reshape(devices * capacity, width)
    return (released, relaid)


def solution(mesh):
    in_specs = (
        P(("region", "unit"), None),
        P(),
        P(("region", "unit"), None),
        P(("region", "unit")),
        P(("region", "unit"), None),
    )
    out_specs = (P(("region", "unit"), None), P(("region", "unit"), None))
    return jax.shard_map(local, mesh=mesh, in_specs=in_specs, out_specs=out_specs, check_vma=False)
```

```python
import jax
import jax.numpy as jnp
from jax import lax
from jax.sharding import PartitionSpec as P

ITERS = 2


step_size = 0.25


def bf16_pieces(value):
    high = lax.reduce_precision(value, exponent_bits=8, mantissa_bits=7)
    rest = value - high
    middle = lax.reduce_precision(rest, exponent_bits=8, mantissa_bits=7)
    low = rest - middle
    return jnp.concatenate(
        [high.astype(jnp.bfloat16), middle.astype(jnp.bfloat16), low.astype(jnp.bfloat16)], axis=0
    )


def one_hot_pick(selector, table_pieces):
    stacked = jnp.concatenate([selector.astype(jnp.bfloat16)] * 3, axis=-1)
    return jnp.einsum("...k,kh->...h", stacked, table_pieces, preferred_element_type=jnp.float32)


def unit_sum(partial, unit_count):
    rows, cols = partial.shape
    grouped = partial.reshape(unit_count, rows // unit_count, cols)
    arrived = lax.all_to_all(grouped, "unit", 0, 0, tiled=True)
    return jnp.sum(arrived, axis=0)


def unit_gather(block, unit_count):
    spread = jnp.broadcast_to(block[None], (unit_count,) + block.shape)
    arrived = lax.all_to_all(spread, "unit", 0, 0, tiled=True)
    return arrived.reshape(unit_count * block.shape[0], block.shape[1])


def local(noisy, strategy, county_hist, tract_county, tract_owner):
    unit_count = lax.axis_size("unit")
    region_count = lax.axis_size("region")
    devices = region_count * unit_count
    tract_rows = noisy.shape[0]
    width = strategy.shape[0]
    county_region = county_hist.shape[0] * unit_count
    first_county = lax.axis_index("region") * county_region
    local_id = tract_county - first_county
    member = (local_id[:, None] == jnp.arange(county_region, dtype=jnp.int32)[None, :]).astype(
        jnp.float32
    )
    county_tally = jnp.sum(member, axis=0)
    tally_lanes = 128
    estimate = jnp.zeros((tract_rows, width), jnp.float32)
    tract_count = None
    for iteration in range(ITERS):
        if iteration == 0:
            misfit = -noisy
        else:
            answers = jnp.dot(
                estimate.astype(jnp.bfloat16), strategy, preferred_element_type=jnp.float32
            )
            misfit = (answers - noisy.astype(jnp.float32)).astype(jnp.bfloat16)
        gradient = lax.dot_general(
            misfit, strategy, (((1,), (1,)), ((), ())), preferred_element_type=jnp.float32
        )
        stepped = estimate - step_size * gradient
        partial_value = lax.dot_general(
            member,
            stepped,
            (((0,), (0,)), ((), ())),
            precision=lax.Precision.HIGHEST,
            preferred_element_type=jnp.float32,
        )
        if tract_count is None:
            tally = jnp.broadcast_to(county_tally[:, None], (county_region, tally_lanes))
            summed = unit_sum(jnp.concatenate([partial_value, tally], axis=1), unit_count)
            child_total = summed[:, :width]
            tract_count = summed[:, width]
        else:
            child_total = unit_sum(partial_value, unit_count)
        if iteration == ITERS - 1:
            late_owner, child_total = lax.optimization_barrier((tract_owner, child_total))
            owners = late_owner[:, 0]
            owner_hits = (
                owners[:, None] == jnp.arange(devices, dtype=jnp.int32)[None, :]
            ).astype(jnp.int32)
            slot_index = jnp.sum(
                (jnp.cumsum(owner_hits, axis=0) - owner_hits) * owner_hits, axis=1
            )
            capacity = 2 * tract_rows // devices
            target = owners * capacity + slot_index
            slot_hits = (
                target[None, :] == jnp.arange(devices * capacity, dtype=jnp.int32)[:, None]
            )
            slot_county = jnp.sum(jnp.where(slot_hits, local_id[None, :] + 1, 0), axis=1) - 1
            half = width // 2
            row_county = jnp.repeat(slot_county, 2)
            pick_shape = (2 * devices * capacity, 2 * 3 * county_region)
            after = jnp.minimum(owners[0], 0)
            row = lax.broadcasted_iota(jnp.int32, pick_shape, 0) + after
            k = lax.broadcasted_iota(jnp.int32, pick_shape, 1) + after
            row_pick = (
                (k // (3 * county_region) == row % 2) & (k % county_region == row_county[:, None])
            ).astype(jnp.bfloat16)
            slot_stepped = (
                jnp.zeros((devices * capacity, width), jnp.float32)
                .at[target]
                .set(stepped)
                .reshape(devices, 2 * capacity, half)
            )
        parent_gap = (county_hist - child_total) / tract_count[:, None]
        region_gap = unit_gather(parent_gap, unit_count)
        estimate = stepped + jnp.dot(
            member, region_gap, precision=lax.Precision.HIGHEST, preferred_element_type=jnp.float32
        )
    high = lax.reduce_precision(region_gap, exponent_bits=8, mantissa_bits=7)
    middle = lax.reduce_precision(region_gap - high, exponent_bits=8, mantissa_bits=7)
    low = (region_gap - high) - middle
    split = [part.astype(jnp.bfloat16) for part in (high, middle, low)]
    halves = jnp.concatenate(
        [part[:, :half] for part in split] + [part[:, half:] for part in split], axis=0
    )
    picked = jnp.dot(row_pick, halves, preferred_element_type=jnp.float32)
    grouped = slot_stepped + picked.reshape(devices, 2 * capacity, half)
    released = jnp.dot(
        estimate.astype(jnp.bfloat16), strategy, preferred_element_type=jnp.float32
    ).astype(jnp.bfloat16)
    arrived = lax.all_to_all(grouped, ("region", "unit"), split_axis=0, concat_axis=0, tiled=True)
    relaid = arrived.reshape(devices * capacity, width)
    return (released, relaid)


def solution(mesh):
    in_specs = (
        P(("region", "unit"), None),
        P(),
        P(("region", "unit"), None),
        P(("region", "unit")),
        P(("region", "unit"), None),
    )
    out_specs = (P(("region", "unit"), None), P(("region", "unit"), None))
    return jax.shard_map(local, mesh=mesh, in_specs=in_specs, out_specs=out_specs, check_vma=False)
```
